512 devices in a mesh: span: 32 (over x, z_lo, core), chord: 16 (over z_hi, y).
Axes of the slice: x: 4, y: 4, z: 16 (z_hi: 4, z_lo: 4; z = z_hi * 4 + z_lo), core: 2. Of those that a mesh axis runs over, the one named last changes fastest.
Arguments:
- adj_rhs: bfloat16 [64, 64, 320, 128], P('span', 'chord'), may hold values from -6 to 6
- diag_inv: bfloat16 [64, 64, 320, 320], P('span', 'chord'), may hold values from -0.3125 to 0.3125
- face_jac: bfloat16 [64, 64, 4, 80, 320], P('span', 'chord'), may hold values from -0.15625 to 0.15625
- face_mask: int32 [64, 64, 4], P('span', 'chord'), may hold values 0 or 1
- wall_map: int32 [64, 64, 16], P('span', 'chord'), may hold values from 0 to 1023
- couple: float32 [6, 5], replicated, may hold values from -3 to 3
- shell_rhs: bfloat16 [32768, 6, 128], P(('span', 'chord')), may hold values from -6 to 6
- shell_inv: float32 [32768, 6, 6], P(('span', 'chord')), may hold values from -2.5 to 2.5
Outputs:
- fluid_adjoint: bfloat16 [64, 64, 320, 128], P('span', 'chord')
- shell_adjoint: bfloat16 [32768, 6, 128], P(('span', 'chord'))
The draws below stay inside these ranges and needn't reach their ends.
All inputs are finite; a program needn't handle non-finite values. No bound on the sum of `face_mask` on one device may be relied on, other than what follows from the above.
Results may differ from the reference program's by a relative error of at most 0.0063.
Values may be sent and summed in bfloat16 or wider, within the bound.
No kernel may reach another device: no remote copies, remote signals or barrier semaphores. Data moves between devices by JAX's collectives and lax.ppermute only.
A program may use at most 64 MiB of HBM per device.

```python
import jax
import jax.numpy as jnp
from jax import lax

NV = 5
NF = 16
SDOF = 6
ITERS = 3
ES = 2
R = 128
BLK = 320
FACE = 80
NSE = 64
NCE = 64
SHELL_COL = 1024
SHELL = 32768


def set_ends(drawn, stream_key, least, largest):
    extent = drawn.shape
    place = [jax.random.randint(jax.random.fold_in(stream_key, axis), (), 0, extent[axis]) for axis in range(len(extent))]
    drawn = drawn.at[tuple(place)].set(least)
    longest = extent.index(max(extent))
    place[longest] = (place[longest] + 1) % extent[longest]
    return drawn.at[tuple(place)].set(largest)


def block_levels(stream_key, dims, cuts, smallest, largest):
    gain, own = 1.0, jax.random.fold_in(stream_key, 6)
    for position, blocks in cuts:
        draws = jnp.exp(jax.random.uniform(jax.random.fold_in(own, position), (blocks,), jnp.float32, smallest / len(cuts), largest / len(cuts)))
        gain = gain * jnp.repeat(draws, dims[position] // blocks).reshape([-1 if axis == position else 1 for axis in range(len(dims))])
    return gain


def scatter_about(rng, extent, spread, most, split=(), held_as=jnp.bfloat16):
    drawn = jax.random.normal(rng, extent, jnp.float32) * spread
    if len(split) > 0:
        drawn = block_levels(rng, extent, split, -0.22, 0.18) * drawn
    return jnp.clip(drawn, min=-most, max=most).astype(held_as)


def setup_inputs(seed: int = 0) -> dict:
    key_of = jax.random.split(jax.random.key(seed), 9)
    adj_rhs = scatter_about(key_of[0], (NSE, NCE, BLK, R), 1.0, 6.0, ((0, 32), (1, 16)))
    diag_inv = scatter_about(key_of[1], (NSE, NCE, BLK, BLK), BLK ** -0.5, 0.3125, ((0, 32), (1, 16)))
    face_jac = scatter_about(key_of[2], (NSE, NCE, 4, FACE, BLK), (4 * BLK) ** -0.5, 0.15625, ((0, 32), (1, 16)))
    face_mask = set_ends((jax.random.randint(key_of[3], (NSE, NCE, 4), 0, 4) < 3).astype(jnp.int32), jax.random.fold_in(key_of[3], 1), 0, 1)
    wall_map = set_ends(jax.random.randint(key_of[4], (NSE, NCE, NF), 0, SHELL_COL), jax.random.fold_in(key_of[4], 1), 0, SHELL_COL - 1).astype(jnp.int32)
    couple = scatter_about(key_of[5], (SDOF, NV), 0.5, 3.0, (), jnp.float32)
    shell_rhs = scatter_about(key_of[6], (SHELL, SDOF, R), 1.0, 6.0, ((0, 512),))
    shell_inv = scatter_about(key_of[7], (SHELL, SDOF, SDOF), SDOF ** -0.5, 2.5, ((0, 512),), jnp.float32)
    return {"adj_rhs": adj_rhs, "diag_inv": diag_inv, "face_jac": face_jac, "face_mask": face_mask, "wall_map": wall_map, "couple": couple, "shell_rhs": shell_rhs, "shell_inv": shell_inv}


def block_apply(mats, vectors):
    def one_row(pair):
        return jnp.einsum('bmn,bnr->bmr', pair[0].astype(jnp.float32), pair[1].astype(jnp.float32))
    return lax.map(one_row, (mats, vectors))


def face_apply(mats, vectors):
    def one_row(pair):
        return jnp.einsum('bdmn,bnr->bdmr', pair[0].astype(jnp.float32), pair[1].astype(jnp.float32))
    return lax.map(one_row, (mats, vectors))


def assemble(adj_rhs, low_span, high_span, low_chord, high_chord, wall_in):
    rows, cols, blk, width = adj_rhs.shape
    resid = adj_rhs.astype(jnp.float32).reshape(rows, cols, 4, 4, 4, NV, width)
    resid = resid.at[:, :, 0].add(-low_span.astype(jnp.float32).reshape(rows, cols, 4, 4, NV, width))
    resid = resid.at[:, :, 3].add(-high_span.astype(jnp.float32).reshape(rows, cols, 4, 4, NV, width))
    resid = resid.at[:, :, :, 0].add(-low_chord.astype(jnp.float32).reshape(rows, cols, 4, 4, NV, width))
    resid = resid.at[:, :, :, 3].add(-high_chord.astype(jnp.float32).reshape(rows, cols, 4, 4, NV, width))
    resid = resid.at[:, :, :, :, 0].add(-wall_in.reshape(rows, cols, 4, 4, NV, width))
    return resid.reshape(rows, cols, blk, width).astype(jnp.bfloat16)


def reference(adj_rhs, diag_inv, face_jac, face_mask, wall_map, couple, shell_rhs, shell_inv):
    high = lax.Precision.HIGHEST
    rows, cols, blk, width = adj_rhs.shape
    fluid = block_apply(diag_inv, adj_rhs).astype(jnp.bfloat16)
    shell = jnp.einsum('nst,ntr->nsr', shell_inv, shell_rhs.astype(jnp.float32), precision=high).astype(jnp.bfloat16)
    strip = (jnp.arange(rows, dtype=jnp.int32) // ES) * SHELL_COL
    shell_ids = (strip[:, None, None] + wall_map).reshape(-1).astype(jnp.int32)
    for step in range(1, ITERS):
        sent = face_apply(face_jac, fluid) * face_mask.astype(jnp.float32)[:, :, :, None, None]
        sent = sent.astype(jnp.bfloat16)
        zero_span = jnp.zeros_like(sent[:1, :, 0])
        zero_chord = jnp.zeros_like(sent[:, :1, 0])
        low_span = jnp.concatenate([zero_span, sent[:-1, :, 0]], 0)
        high_span = jnp.concatenate([sent[1:, :, 1], zero_span], 0)
        low_chord = jnp.concatenate([zero_chord, sent[:, :-1, 2]], 1)
        high_chord = jnp.concatenate([sent[:, 1:, 3], zero_chord], 1)
        picked = shell[shell_ids].astype(jnp.float32)
        wall_in = jnp.einsum('sv,wsr->wvr', couple, picked, precision=high)
        fluid_wall = fluid.reshape(rows, cols, 4, 4, 4, NV, width)[:, :, :, :, 0].reshape(rows * cols * NF, NV, width)
        pushed = jnp.einsum('sv,wvr->wsr', couple, fluid_wall.astype(jnp.float32), precision=high)
        shell_load = jnp.zeros((SHELL, SDOF, width), jnp.float32).at[shell_ids].add(pushed)
        resid = assemble(adj_rhs, low_span, high_span, low_chord, high_chord, wall_in)
        fluid = block_apply(diag_inv, resid).astype(jnp.bfloat16)
        shell = jnp.einsum('nst,ntr->nsr', shell_inv, shell_rhs.astype(jnp.float32) - shell_load, precision=high).astype(jnp.bfloat16)
    return fluid, shell
```

```python
import jax
import jax.numpy as jnp
from jax import lax
from jax.sharding import PartitionSpec as P

NV = 5
ITERS = 3
CY = 4


def passed_along(block, axis, distance):
    devices = range(lax.axis_size(axis))
    route = [(i - distance, i) for i in devices if i - distance in devices]
    return lax.ppermute(block, axis, route)


def chord_shift(block, dz, dy):
    size = lax.axis_size("chord")
    cz = size // CY
    route = [
        (c, ((c // CY + dz) % cz) * CY + (c % CY + dy) % CY) for c in range(size)
    ]
    return lax.ppermute(block, "chord", route)


def assemble(adj_rhs, low_span, high_span, low_chord, high_chord, wall_in):
    rows, cols, blk, width = adj_rhs.shape
    resid = adj_rhs.astype(jnp.float32).reshape(rows, cols, 4, 4, 4, NV, width)
    resid = resid.at[:, :, 0].add(
        -low_span.astype(jnp.float32).reshape(rows, cols, 4, 4, NV, width)
    )
    resid = resid.at[:, :, 3].add(
        -high_span.astype(jnp.float32).reshape(rows, cols, 4, 4, NV, width)
    )
    resid = resid.at[:, :, :, 0].add(
        -low_chord.astype(jnp.float32).reshape(rows, cols, 4, 4, NV, width)
    )
    resid = resid.at[:, :, :, 3].add(
        -high_chord.astype(jnp.float32).reshape(rows, cols, 4, 4, NV, width)
    )
    resid = resid.at[:, :, :, :, 0].add(-wall_in.reshape(rows, cols, 4, 4, NV, width))
    return resid.reshape(rows, cols, blk, width).astype(jnp.bfloat16)


def pass_span(moving, offset):
    rim_row = moving[-1:] if offset == 1 else moving[:1]
    arrived = passed_along(rim_row, "span", offset)
    if offset == 1:
        return jnp.concatenate([arrived, moving[:-1]], 0)
    return jnp.concatenate([moving[1:], arrived], 0)


def pass_chord(moving, offset):
    rim_col = moving[:, -1:] if offset == 1 else moving[:, :1]
    arrived = passed_along(rim_col, "chord", offset)
    if offset == 1:
        return jnp.concatenate([arrived, moving[:, :-1]], 1)
    return jnp.concatenate([moving[:, 1:], arrived], 1)


def face_terms(sent):
    low_span = pass_span(sent[:, :, 0], 1)
    high_span = pass_span(sent[:, :, 1], -1)
    low_chord = pass_chord(sent[:, :, 2], 1)
    high_chord = pass_chord(sent[:, :, 3], -1)
    return (low_span, high_span, low_chord, high_chord)


def gather_strip(shell):
    cz = lax.axis_size("chord") // CY
    first = jnp.stack([shell] + [chord_shift(shell, k, 0) for k in range(1, cz)])
    return jnp.stack([first] + [chord_shift(first, 0, k) for k in range(1, CY)])


def reduce_strip(partial):
    cz = partial.shape[1]
    part = partial[0]
    for k in range(1, CY):
        part = part + chord_shift(partial[k], 0, k)
    total = part[0]
    for k in range(1, cz):
        total = total + chord_shift(part[k], k, 0)
    return total


def per_device(adj_rhs, diag_inv, face_jac, face_mask, wall_map, couple, shell_rhs, shell_inv):
    high = lax.Precision.HIGHEST
    rows, cols, blk, width = adj_rhs.shape
    shell_count = shell_rhs.shape[0]
    size = lax.axis_size("chord")
    cz = size // CY
    chord_pos = lax.axis_index("chord")
    zpos = chord_pos // CY
    ypos = chord_pos % CY
    wall_local = wall_map.reshape(-1)
    wall_count = wall_local.shape[0]
    node = lax.iota(jnp.int32, shell_count)
    ky = lax.iota(jnp.int32, CY)[:, None, None]
    kz = lax.iota(jnp.int32, cz)[None, :, None]
    got_ids = ((((zpos - kz) % cz) * CY + (ypos - ky) % CY) * shell_count + node).reshape(-1)
    out_ids = ((((zpos + kz) % cz) * CY + (ypos + ky) % CY) * shell_count + node).reshape(-1)
    pick_hit = (wall_local[:, None] == got_ids[None, :]).astype(jnp.bfloat16)
    load_hit = (out_ids[:, None] == wall_local[None, :]).astype(jnp.bfloat16)
    fluid = jnp.einsum(
        "abmn,abnr->abmr", diag_inv, adj_rhs, preferred_element_type=jnp.float32
    ).astype(jnp.bfloat16)
    shell = jnp.einsum(
        "nst,ntr->nsr", shell_inv, shell_rhs.astype(jnp.float32), precision=high
    ).astype(jnp.bfloat16)
    weights = face_mask.astype(jnp.float32)[:, :, :, None, None]
    sdof = shell.shape[1]
    for step in range(1, ITERS):
        sent = jnp.einsum("abdmn,abnr->abdmr", face_jac, fluid, preferred_element_type=jnp.float32)
        sent = (sent * weights).astype(jnp.bfloat16)
        low_span, high_span, low_chord, high_chord = face_terms(sent)
        strip = gather_strip(shell).reshape(size * shell_count, sdof * width)
        picked = jnp.dot(pick_hit, strip, preferred_element_type=jnp.float32)
        wall_in = jnp.einsum(
            "sv,wsr->wvr", couple, picked.reshape(wall_count, sdof, width), precision=high
        )
        wall_rows = fluid.reshape(rows, cols, 4, 4, 4, NV, width)[:, :, :, :, 0].reshape(
            wall_count, NV * width
        )
        partial = jnp.dot(load_hit, wall_rows, preferred_element_type=jnp.float32)
        summed = reduce_strip(partial.reshape(CY, cz, shell_count, NV, width))
        shell_load = jnp.einsum("sv,nvr->nsr", couple, summed, precision=high)
        resid = assemble(adj_rhs, low_span, high_span, low_chord, high_chord, wall_in)
        fluid = jnp.einsum(
            "abmn,abnr->abmr", diag_inv, resid, preferred_element_type=jnp.float32
        ).astype(jnp.bfloat16)
        shell = jnp.einsum(
            "nst,ntr->nsr", shell_inv, shell_rhs.astype(jnp.float32) - shell_load, precision=high
        ).astype(jnp.bfloat16)
    return (fluid, shell)


def solution(mesh):
    return jax.shard_map(
        per_device,
        mesh=mesh,
        in_specs=(
            P("span", "chord", None, None),
            P("span", "chord", None, None),
            P("span", "chord", None, None, None),
            P("span", "chord", None),
            P("span", "chord", None),
            P(),
            P(("span", "chord"), None, None),
            P(("span", "chord"), None, None),
        ),
        out_specs=(P("span", "chord", None, None), P(("span", "chord"), None, None)),
        check_vma=False,
    )
```

```python
import jax
import jax.numpy as jnp
from jax import lax
from jax.sharding import PartitionSpec as P

NV = 5
ITERS = 3
CY = 4


def passed_along(block, axis, distance):
    devices = range(lax.axis_size(axis))
    route = [(i - distance, i) for i in devices if i - distance in devices]
    return lax.ppermute(block, axis, route)


def chord_shift(block, dz, dy):
    size = lax.axis_size("chord")
    cz = size // CY
    route = [
        (c, ((c // CY + dz) % cz) * CY + (c % CY + dy) % CY) for c in range(size)
    ]
    return lax.ppermute(block, "chord", route)


def assemble(adj_rhs, low_span, high_span, low_chord, high_chord, wall_in):
    rows, cols, blk, width = adj_rhs.shape
    resid = adj_rhs.astype(jnp.float32).reshape(rows, cols, 4, 4, 4, NV, width)
    resid = resid.at[:, :, 0].add(
        -low_span.astype(jnp.float32).reshape(rows, cols, 4, 4, NV, width)
    )
    resid = resid.at[:, :, 3].add(
        -high_span.astype(jnp.float32).reshape(rows, cols, 4, 4, NV, width)
    )
    resid = resid.at[:, :, :, 0].add(
        -low_chord.astype(jnp.float32).reshape(rows, cols, 4, 4, NV, width)
    )
    resid = resid.at[:, :, :, 3].add(
        -high_chord.astype(jnp.float32).reshape(rows, cols, 4, 4, NV, width)
    )
    resid = resid.at[:, :, :, :, 0].add(-wall_in.reshape(rows, cols, 4, 4, NV, width))
    return resid.reshape(rows, cols, blk, width).astype(jnp.bfloat16)


def pass_span(moving, offset):
    rim_row = moving[-1:] if offset == 1 else moving[:1]
    arrived = passed_along(rim_row, "span", offset)
    if offset == 1:
        return jnp.concatenate([arrived, moving[:-1]], 0)
    return jnp.concatenate([moving[1:], arrived], 0)


def pass_chord(moving, offset):
    rim_col = moving[:, -1:] if offset == 1 else moving[:, :1]
    arrived = passed_along(rim_col, "chord", offset)
    if offset == 1:
        return jnp.concatenate([arrived, moving[:, :-1]], 1)
    return jnp.concatenate([moving[:, 1:], arrived], 1)


def face_terms(sent):
    low_span = pass_span(sent[:, :, 0], 1)
    high_span = pass_span(sent[:, :, 1], -1)
    low_chord = pass_chord(sent[:, :, 2], 1)
    high_chord = pass_chord(sent[:, :, 3], -1)
    return (low_span, high_span, low_chord, high_chord)


def gather_strip(shell):
    cz = lax.axis_size("chord") // CY
    first = jnp.stack([shell] + [chord_shift(shell, k, 0) for k in range(1, cz)])
    return jnp.stack([first] + [chord_shift(first, 0, k) for k in range(1, CY)])


def reduce_strip(partial):
    cz = partial.shape[1]
    part = partial[0]
    for k in range(1, CY):
        part = part + chord_shift(partial[k], 0, k)
    total = part[0]
    for k in range(1, cz):
        total = total + chord_shift(part[k], k, 0)
    return total


def per_device(adj_rhs, diag_inv, face_jac, face_mask, wall_map, couple, shell_rhs, shell_inv):
    high = lax.Precision.HIGHEST
    rows, cols, blk, width = adj_rhs.shape
    shell_count = shell_rhs.shape[0]
    size = lax.axis_size("chord")
    cz = size // CY
    chord_pos = lax.axis_index("chord")
    zpos = chord_pos // CY
    ypos = chord_pos % CY
    wall_local = wall_map.reshape(-1)
    wall_count = wall_local.shape[0]
    node = lax.iota(jnp.int32, shell_count)
    ky = lax.iota(jnp.int32, CY)[:, None, None]
    kz = lax.iota(jnp.int32, cz)[None, :, None]
    got_ids = ((((zpos - kz) % cz) * CY + (ypos - ky) % CY) * shell_count + node).reshape(-1)
    out_ids = ((((zpos + kz) % cz) * CY + (ypos + ky) % CY) * shell_count + node).reshape(-1)
    pick_hit = (wall_local[:, None] == got_ids[None, :]).astype(jnp.bfloat16)
    load_hit = (out_ids[:, None] == wall_local[None, :]).astype(jnp.bfloat16)
    fluid = jnp.einsum(
        "abmn,abnr->abmr", diag_inv, adj_rhs, preferred_element_type=jnp.float32
    ).astype(jnp.bfloat16)
    shell = jnp.einsum(
        "nst,ntr->nsr", shell_inv, shell_rhs.astype(jnp.float32), precision=high
    ).astype(jnp.bfloat16)
    weights = face_mask.astype(jnp.float32)[:, :, :, None, None]
    sdof = shell.shape[1]
    for step in range(1, ITERS):
        sent = jnp.einsum("abdmn,abnr->abdmr", face_jac, fluid, preferred_element_type=jnp.float32)
        sent = (sent * weights).astype(jnp.bfloat16)
        low_span, high_span, low_chord, high_chord = face_terms(sent)
        strip = gather_strip(shell.reshape(shell_count, sdof * width))
        strip = strip.reshape(size * shell_count, sdof * width)
        picked = jnp.dot(pick_hit, strip, preferred_element_type=jnp.float32)
        wall_in = jnp.einsum(
            "sv,wsr->wvr", couple, picked.reshape(wall_count, sdof, width), precision=high
        )
        wall_rows = fluid.reshape(rows, cols, 4, 4, 4, NV, width)[:, :, :, :, 0].reshape(
            wall_count, NV * width
        )
        partial = jnp.dot(load_hit, wall_rows, preferred_element_type=jnp.float32)
        summed = reduce_strip(partial.reshape(CY, cz, shell_count, NV * width))
        shell_load = jnp.einsum(
            "sv,nvr->nsr", couple, summed.reshape(shell_count, NV, width), precision=high
        )
        resid = assemble(adj_rhs, low_span, high_span, low_chord, high_chord, wall_in)
        fluid = jnp.einsum(
            "abmn,abnr->abmr", diag_inv, resid, preferred_element_type=jnp.float32
        ).astype(jnp.bfloat16)
        shell = jnp.einsum(
            "nst,ntr->nsr", shell_inv, shell_rhs.astype(jnp.float32) - shell_load, precision=high
        ).astype(jnp.bfloat16)
    return (fluid, shell)


def solution(mesh):
    return jax.shard_map(
        per_device,
        mesh=mesh,
        in_specs=(
            P("span", "chord", None, None),
            P("span", "chord", None, None),
            P("span", "chord", None, None, None),
            P("span", "chord", None),
            P("span", "chord", None),
            P(),
            P(("span", "chord"), None, None),
            P(("span", "chord"), None, None),
        ),
        out_specs=(P("span", "chord", None, None), P(("span", "chord"), None, None)),
        check_vma=False,
    )
```

```python
import jax
import jax.numpy as jnp
from jax import lax
from jax.sharding import PartitionSpec as P

NV = 5
ITERS = 3
CY = 4


def passed_along(block, axis, distance):
    devices = range(lax.axis_size(axis))
    route = [(i - distance, i) for i in devices if i - distance in devices]
    return lax.ppermute(block, axis, route)


def chord_shift(block, dz, dy):
    size = lax.axis_size("chord")
    cz = size // CY
    route = [
        (c, ((c // CY + dz) % cz) * CY + (c % CY + dy) % CY) for c in range(size)
    ]
    return lax.ppermute(block, "chord", route)


def assemble(adj_rhs, low_span, high_span, low_chord, high_chord, wall_in):
    rows, cols, blk, width = adj_rhs.shape
    resid = adj_rhs.astype(jnp.float32).reshape(rows, cols, 4, 4, 4, NV, width)
    resid = resid.at[:, :, 0].add(
        -low_span.astype(jnp.float32).reshape(rows, cols, 4, 4, NV, width)
    )
    resid = resid.at[:, :, 3].add(
        -high_span.astype(jnp.float32).reshape(rows, cols, 4, 4, NV, width)
    )
    resid = resid.at[:, :, :, 0].add(
        -low_chord.astype(jnp.float32).reshape(rows, cols, 4, 4, NV, width)
    )
    resid = resid.at[:, :, :, 3].add(
        -high_chord.astype(jnp.float32).reshape(rows, cols, 4, 4, NV, width)
    )
    resid = resid.at[:, :, :, :, 0].add(-wall_in.reshape(rows, cols, 4, 4, NV, width))
    return resid.reshape(rows, cols, blk, width).astype(jnp.bfloat16)


def pass_span(moving, offset):
    rim_row = moving[-1:] if offset == 1 else moving[:1]
    arrived = passed_along(rim_row, "span", offset)
    if offset == 1:
        return jnp.concatenate([arrived, moving[:-1]], 0)
    return jnp.concatenate([moving[1:], arrived], 0)


def pass_chord(moving, offset):
    rim_col = moving[:, -1:] if offset == 1 else moving[:, :1]
    arrived = passed_along(rim_col, "chord", offset)
    if offset == 1:
        return jnp.concatenate([arrived, moving[:, :-1]], 1)
    return jnp.concatenate([moving[:, 1:], arrived], 1)


def face_terms(sent):
    low_span = pass_span(sent[:, :, 0], 1)
    high_span = pass_span(sent[:, :, 1], -1)
    low_chord = pass_chord(sent[:, :, 2], 1)
    high_chord = pass_chord(sent[:, :, 3], -1)
    return (low_span, high_span, low_chord, high_chord)


def over_y(block):
    return [block] + [chord_shift(block, 0, k) for k in range(1, CY)]


def over_z(block):
    cz = lax.axis_size("chord") // CY
    return [block] + [chord_shift(block, k, 0) for k in range(1, cz)]


def per_device(adj_rhs, diag_inv, face_jac, face_mask, wall_map, couple, shell_rhs, shell_inv):
    high = lax.Precision.HIGHEST
    rows, cols, blk, width = adj_rhs.shape
    shell_count = shell_rhs.shape[0]
    size = lax.axis_size("chord")
    cz = size // CY
    chord_pos = lax.axis_index("chord")
    zpos = chord_pos // CY
    ypos = chord_pos % CY
    wall_local = wall_map.reshape(-1)
    wall_count = wall_local.shape[0]
    node = lax.iota(jnp.int32, shell_count)
    kz = lax.iota(jnp.int32, cz)[:, None]
    got_ids = ((((zpos - kz) % cz) * CY + ypos) * shell_count + node).reshape(-1)
    out_ids = ((((zpos + kz) % cz) * CY + ypos) * shell_count + node).reshape(-1)
    maps_to = [wall_local] + [chord_shift(wall_local, 0, -k) for k in range(1, CY)]
    maps_from = jnp.concatenate(over_y(wall_local))
    pick_hits = [(m[:, None] == got_ids[None, :]).astype(jnp.bfloat16) for m in maps_to]
    load_hit = (out_ids[:, None] == maps_from[None, :]).astype(jnp.bfloat16)
    fluid = jnp.einsum(
        "abmn,abnr->abmr", diag_inv, adj_rhs, preferred_element_type=jnp.float32
    ).astype(jnp.bfloat16)
    shell = jnp.einsum(
        "nst,ntr->nsr", shell_inv, shell_rhs.astype(jnp.float32), precision=high
    ).astype(jnp.bfloat16)
    weights = face_mask.astype(jnp.float32)[:, :, :, None, None]
    sdof = shell.shape[1]
    for step in range(1, ITERS):
        sent = jnp.einsum("abdmn,abnr->abdmr", face_jac, fluid, preferred_element_type=jnp.float32)
        sent = (sent * weights).astype(jnp.bfloat16)
        low_span, high_span, low_chord, high_chord = face_terms(sent)
        column = jnp.concatenate(over_z(shell.reshape(shell_count, sdof * width)))
        served = [
            jnp.dot(h, column, preferred_element_type=jnp.float32).astype(jnp.bfloat16)
            for h in pick_hits
        ]
        picked = served[0].astype(jnp.float32)
        for k in range(1, CY):
            picked = picked + chord_shift(served[k], 0, k).astype(jnp.float32)
        wall_in = jnp.einsum(
            "sv,wsr->wvr", couple, picked.reshape(wall_count, sdof, width), precision=high
        )
        wall_rows = fluid.reshape(rows, cols, 4, 4, 4, NV, width)[:, :, :, :, 0].reshape(
            wall_count, NV * width
        )
        row_group = jnp.concatenate(over_y(wall_rows))
        partial = jnp.dot(load_hit, row_group, preferred_element_type=jnp.float32)
        partial = partial.reshape(cz, shell_count, NV * width)
        summed = partial[0]
        for k in range(1, cz):
            summed = summed + chord_shift(partial[k], k, 0)
        shell_load = jnp.einsum(
            "sv,nvr->nsr", couple, summed.reshape(shell_count, NV, width), precision=high
        )
        resid = assemble(adj_rhs, low_span, high_span, low_chord, high_chord, wall_in)
        fluid = jnp.einsum(
            "abmn,abnr->abmr", diag_inv, resid, preferred_element_type=jnp.float32
        ).astype(jnp.bfloat16)
        shell = jnp.einsum(
            "nst,ntr->nsr", shell_inv, shell_rhs.astype(jnp.float32) - shell_load, precision=high
        ).astype(jnp.bfloat16)
    return (fluid, shell)


def solution(mesh):
    return jax.shard_map(
        per_device,
        mesh=mesh,
        in_specs=(
            P("span", "chord", None, None),
            P("span", "chord", None, None),
            P("span", "chord", None, None, None),
            P("span", "chord", None),
            P("span", "chord", None),
            P(),
            P(("span", "chord"), None, None),
            P(("span", "chord"), None, None),
        ),
        out_specs=(P("span", "chord", None, None), P(("span", "chord"), None, None)),
        check_vma=False,
    )
```

```python
import jax
import jax.numpy as jnp
from jax import lax
from jax.sharding import PartitionSpec as P

NV = 5
ITERS = 3
CY = 4


def passed_along(block, axis, distance):
    devices = range(lax.axis_size(axis))
    route = [(i - distance, i) for i in devices if i - distance in devices]
    return lax.ppermute(block, axis, route)


def chord_shift(block, dz, dy):
    size = lax.axis_size("chord")
    cz = size // CY
    route = [
        (c, ((c // CY + dz) % cz) * CY + (c % CY + dy) % CY) for c in range(size)
    ]
    return lax.ppermute(block, "chord", route)


def assemble(adj_rhs, low_span, high_span, low_chord, high_chord, wall_in):
    rows, cols, blk, width = adj_rhs.shape
    resid = adj_rhs.astype(jnp.float32).reshape(rows, cols, 4, 4, 4, NV, width)
    resid = resid.at[:, :, 0].add(
        -low_span.astype(jnp.float32).reshape(rows, cols, 4, 4, NV, width)
    )
    resid = resid.at[:, :, 3].add(
        -high_span.astype(jnp.float32).reshape(rows, cols, 4, 4, NV, width)
    )
    resid = resid.at[:, :, :, 0].add(
        -low_chord.astype(jnp.float32).reshape(rows, cols, 4, 4, NV, width)
    )
    resid = resid.at[:, :, :, 3].add(
        -high_chord.astype(jnp.float32).reshape(rows, cols, 4, 4, NV, width)
    )
    resid = resid.at[:, :, :, :, 0].add(-wall_in.reshape(rows, cols, 4, 4, NV, width))
    return resid.reshape(rows, cols, blk, width).astype(jnp.bfloat16)


def pass_span(moving, offset):
    rim_row = moving[-1:] if offset == 1 else moving[:1]
    arrived = passed_along(rim_row, "span", offset)
    if offset == 1:
        return jnp.concatenate([arrived, moving[:-1]], 0)
    return jnp.concatenate([moving[1:], arrived], 0)


def pass_chord(moving, offset):
    rim_col = moving[:, -1:] if offset == 1 else moving[:, :1]
    arrived = passed_along(rim_col, "chord", offset)
    if offset == 1:
        return jnp.concatenate([arrived, moving[:, :-1]], 1)
    return jnp.concatenate([moving[:, 1:], arrived], 1)


def face_terms(sent):
    low_span = pass_span(sent[:, :, 0], 1)
    high_span = pass_span(sent[:, :, 1], -1)
    low_chord = pass_chord(sent[:, :, 2], 1)
    high_chord = pass_chord(sent[:, :, 3], -1)
    return (low_span, high_span, low_chord, high_chord)


def over_y(block):
    return [block] + [chord_shift(block, 0, k) for k in range(1, CY)]


def over_z(block):
    cz = lax.axis_size("chord") // CY
    return [block] + [chord_shift(block, k, 0) for k in range(1, cz)]


def per_device(adj_rhs, diag_inv, face_jac, face_mask, wall_map, couple, shell_rhs, shell_inv):
    high = lax.Precision.HIGHEST
    rows, cols, blk, width = adj_rhs.shape
    shell_count = shell_rhs.shape[0]
    size = lax.axis_size("chord")
    cz = size // CY
    chord_pos = lax.axis_index("chord")
    zpos = chord_pos // CY
    ypos = chord_pos % CY
    wall_local = wall_map.reshape(-1)
    wall_count = wall_local.shape[0]
    node = lax.iota(jnp.int32, shell_count)
    kz = lax.iota(jnp.int32, cz)[:, None]
    ky = lax.iota(jnp.int32, CY)[:, None]
    got_ids = ((((zpos - kz) % cz) * CY + ypos) * shell_count + node).reshape(-1)
    out_ids = ((zpos * CY + (ypos + ky) % CY) * shell_count + node).reshape(-1)
    maps_to = [wall_local] + [chord_shift(wall_local, 0, -k) for k in range(1, CY)]
    maps_from = jnp.concatenate(over_z(wall_local))
    pick_hits = [(m[:, None] == got_ids[None, :]).astype(jnp.bfloat16) for m in maps_to]
    load_hit = (out_ids[:, None] == maps_from[None, :]).astype(jnp.bfloat16)
    fluid = jnp.einsum(
        "abmn,abnr->abmr", diag_inv, adj_rhs, preferred_element_type=jnp.float32
    ).astype(jnp.bfloat16)
    shell = jnp.einsum(
        "nst,ntr->nsr", shell_inv, shell_rhs.astype(jnp.float32), precision=high
    ).astype(jnp.bfloat16)
    weights = face_mask.astype(jnp.float32)[:, :, :, None, None]
    sdof = shell.shape[1]
    for step in range(1, ITERS):
        sent = jnp.einsum("abdmn,abnr->abdmr", face_jac, fluid, preferred_element_type=jnp.float32)
        sent = (sent * weights).astype(jnp.bfloat16)
        low_span, high_span, low_chord, high_chord = face_terms(sent)
        wall_rows = fluid.reshape(rows, cols, 4, 4, 4, NV, width)[:, :, :, :, 0].reshape(
            wall_count * NV, width
        )
        shell_rows = shell.reshape(shell_count * sdof, width)
        cut = shell_count * sdof
        arrived = over_z(jnp.concatenate([shell_rows, wall_rows]))
        column = jnp.concatenate(
            [a[:cut].reshape(shell_count, sdof * width) for a in arrived]
        )
        row_group = jnp.concatenate(
            [a[cut:].reshape(wall_count, NV * width) for a in arrived]
        )
        partial = jnp.dot(load_hit, row_group, preferred_element_type=jnp.float32)
        partial = partial.reshape(CY, shell_count * NV, width)
        packs = [
            jnp.concatenate(
                [
                    jnp.dot(h, column, preferred_element_type=jnp.float32).reshape(
                        wall_count * sdof, width
                    ),
                    partial[k],
                ]
            )
            for k, h in enumerate(pick_hits)
        ]
        total = packs[0]
        for k in range(1, CY):
            total = total + chord_shift(packs[k], 0, k)
        picked = total[: wall_count * sdof].reshape(wall_count, sdof, width)
        summed = total[wall_count * sdof :].reshape(shell_count, NV, width)
        wall_in = jnp.einsum("sv,wsr->wvr", couple, picked, precision=high)
        shell_load = jnp.einsum("sv,nvr->nsr", couple, summed, precision=high)
        resid = assemble(adj_rhs, low_span, high_span, low_chord, high_chord, wall_in)
        fluid = jnp.einsum(
            "abmn,abnr->abmr", diag_inv, resid, preferred_element_type=jnp.float32
        ).astype(jnp.bfloat16)
        shell = jnp.einsum(
            "nst,ntr->nsr", shell_inv, shell_rhs.astype(jnp.float32) - shell_load, precision=high
        ).astype(jnp.bfloat16)
    return (fluid, shell)


def solution(mesh):
    return jax.shard_map(
        per_device,
        mesh=mesh,
        in_specs=(
            P("span", "chord", None, None),
            P("span", "chord", None, None),
            P("span", "chord", None, None, None),
            P("span", "chord", None),
            P("span", "chord", None),
            P(),
            P(("span", "chord"), None, None),
            P(("span", "chord"), None, None),
        ),
        out_specs=(P("span", "chord", None, None), P(("span", "chord"), None, None)),
        check_vma=False,
    )
```

```python
import jax
import jax.numpy as jnp
from jax import lax
from jax.sharding import PartitionSpec as P

NV = 5
ITERS = 3
CY = 4


def passed_along(block, axis, distance):
    devices = range(lax.axis_size(axis))
    route = [(i - distance, i) for i in devices if i - distance in devices]
    return lax.ppermute(block, axis, route)


def chord_shift(block, dz, dy):
    size = lax.axis_size("chord")
    cz = size // CY
    route = [
        (c, ((c // CY + dz) % cz) * CY + (c % CY + dy) % CY) for c in range(size)
    ]
    return lax.ppermute(block, "chord", route)


def assemble(adj_rhs, low_span, high_span, low_chord, high_chord, wall_in):
    rows, cols, blk, width = adj_rhs.shape
    resid = adj_rhs.astype(jnp.float32).reshape(rows, cols, 4, 4, 4, NV, width)
    resid = resid.at[:, :, 0].add(
        -low_span.astype(jnp.float32).reshape(rows, cols, 4, 4, NV, width)
    )
    resid = resid.at[:, :, 3].add(
        -high_span.astype(jnp.float32).reshape(rows, cols, 4, 4, NV, width)
    )
    resid = resid.at[:, :, :, 0].add(
        -low_chord.astype(jnp.float32).reshape(rows, cols, 4, 4, NV, width)
    )
    resid = resid.at[:, :, :, 3].add(
        -high_chord.astype(jnp.float32).reshape(rows, cols, 4, 4, NV, width)
    )
    resid = resid.at[:, :, :, :, 0].add(-wall_in.reshape(rows, cols, 4, 4, NV, width))
    return resid.reshape(rows, cols, blk, width).astype(jnp.bfloat16)


def pass_span(moving, offset):
    rim_row = moving[-1:] if offset == 1 else moving[:1]
    arrived = passed_along(rim_row, "span", offset)
    if offset == 1:
        return jnp.concatenate([arrived, moving[:-1]], 0)
    return jnp.concatenate([moving[1:], arrived], 0)


def pass_chord(moving, offset):
    rim_col = moving[:, -1:] if offset == 1 else moving[:, :1]
    arrived = passed_along(rim_col, "chord", offset)
    if offset == 1:
        return jnp.concatenate([arrived, moving[:, :-1]], 1)
    return jnp.concatenate([moving[:, 1:], arrived], 1)


def face_terms(sent):
    low_span = pass_span(sent[:, :, 0], 1)
    high_span = pass_span(sent[:, :, 1], -1)
    low_chord = pass_chord(sent[:, :, 2], 1)
    high_chord = pass_chord(sent[:, :, 3], -1)
    return (low_span, high_span, low_chord, high_chord)


def over_y(block):
    return [block] + [chord_shift(block, 0, k) for k in range(1, CY)]


def over_z(block):
    cz = lax.axis_size("chord") // CY
    return [block] + [chord_shift(block, k, 0) for k in range(1, cz)]


def per_device(adj_rhs, diag_inv, face_jac, face_mask, wall_map, couple, shell_rhs, shell_inv):
    high = lax.Precision.HIGHEST
    rows, cols, blk, width = adj_rhs.shape
    shell_count = shell_rhs.shape[0]
    size = lax.axis_size("chord")
    cz = size // CY
    chord_pos = lax.axis_index("chord")
    zpos = chord_pos // CY
    ypos = chord_pos % CY
    wall_local = wall_map.reshape(-1)
    wall_count = wall_local.shape[0]
    node = lax.iota(jnp.int32, shell_count)
    none_s = jnp.full((shell_count,), -1, jnp.int32)
    none_w = jnp.full((wall_count,), -1, jnp.int32)
    held = over_z(wall_local)
    col_s = jnp.concatenate(
        [
            jnp.concatenate([(((zpos - k) % cz) * CY + ypos) * shell_count + node, none_w])
            for k in range(cz)
        ]
    )
    col_w = jnp.concatenate([jnp.concatenate([none_s, held[k]]) for k in range(cz)])
    maps_to = [wall_local] + [chord_shift(wall_local, 0, -k) for k in range(1, CY)]
    hits = []
    for k in range(CY):
        want_s = jnp.concatenate([maps_to[k], none_s - 1])
        owner = (zpos * CY + (ypos + k) % CY) * shell_count + node
        want_w = jnp.concatenate([none_w - 1, owner])
        hit = (want_s[:, None] == col_s[None, :]) | (want_w[:, None] == col_w[None, :])
        hits.append(hit.astype(jnp.bfloat16))
    fluid = jnp.einsum(
        "abmn,abnr->abmr", diag_inv, adj_rhs, preferred_element_type=jnp.float32
    ).astype(jnp.bfloat16)
    shell = jnp.einsum(
        "nst,ntr->nsr", shell_inv, shell_rhs.astype(jnp.float32), precision=high
    ).astype(jnp.bfloat16)
    weights = face_mask.astype(jnp.float32)[:, :, :, None, None]
    sdof = shell.shape[1]
    for step in range(1, ITERS):
        sent = jnp.einsum("abdmn,abnr->abdmr", face_jac, fluid, preferred_element_type=jnp.float32)
        sent = (sent * weights).astype(jnp.bfloat16)
        low_span, high_span, low_chord, high_chord = face_terms(sent)
        wall_rows = fluid.reshape(rows, cols, 4, 4, 4, NV, width)[:, :, :, :, 0].reshape(
            wall_count, NV * width
        )
        wall_rows = jnp.pad(wall_rows, ((0, 0), (0, (sdof - NV) * width)))
        block = jnp.concatenate([shell.reshape(shell_count, sdof * width), wall_rows])
        column = jnp.concatenate(over_z(block))
        served = [jnp.dot(h, column, preferred_element_type=jnp.float32) for h in hits]
        total = served[0]
        for k in range(1, CY):
            total = total + chord_shift(served[k], 0, k)
        picked = total[:wall_count].reshape(wall_count, sdof, width)
        summed = total[wall_count:, : NV * width].reshape(shell_count, NV, width)
        wall_in = jnp.einsum("sv,wsr->wvr", couple, picked, precision=high)
        shell_load = jnp.einsum("sv,nvr->nsr", couple, summed, precision=high)
        resid = assemble(adj_rhs, low_span, high_span, low_chord, high_chord, wall_in)
        fluid = jnp.einsum(
            "abmn,abnr->abmr", diag_inv, resid, preferred_element_type=jnp.float32
        ).astype(jnp.bfloat16)
        shell = jnp.einsum(
            "nst,ntr->nsr", shell_inv, shell_rhs.astype(jnp.float32) - shell_load, precision=high
        ).astype(jnp.bfloat16)
    return (fluid, shell)


def solution(mesh):
    return jax.shard_map(
        per_device,
        mesh=mesh,
        in_specs=(
            P("span", "chord", None, None),
            P("span", "chord", None, None),
            P("span", "chord", None, None, None),
            P("span", "chord", None),
            P("span", "chord", None),
            P(),
            P(("span", "chord"), None, None),
            P(("span", "chord"), None, None),
        ),
        out_specs=(P("span", "chord", None, None), P(("span", "chord"), None, None)),
        check_vma=False,
    )
```

```python
import jax
import jax.numpy as jnp
from jax import lax
from jax.sharding import PartitionSpec as P

NV = 5
ITERS = 3
CY = 4


def passed_along(block, axis, distance):
    devices = range(lax.axis_size(axis))
    route = [(i - distance, i) for i in devices if i - distance in devices]
    return lax.ppermute(block, axis, route)


def chord_shift(block, dz, dy):
    size = lax.axis_size("chord")
    cz = size // CY
    route = [
        (c, ((c // CY + dz) % cz) * CY + (c % CY + dy) % CY) for c in range(size)
    ]
    return lax.ppermute(block, "chord", route)


def assemble(adj_rhs, low_span, high_span, low_chord, high_chord, wall_in):
    rows, cols, blk, width = adj_rhs.shape
    resid = adj_rhs.astype(jnp.float32).reshape(rows, cols, 4, 4, 4, NV, width)
    resid = resid.at[:, :, 0].add(
        -low_span.astype(jnp.float32).reshape(rows, cols, 4, 4, NV, width)
    )
    resid = resid.at[:, :, 3].add(
        -high_span.astype(jnp.float32).reshape(rows, cols, 4, 4, NV, width)
    )
    resid = resid.at[:, :, :, 0].add(
        -low_chord.astype(jnp.float32).reshape(rows, cols, 4, 4, NV, width)
    )
    resid = resid.at[:, :, :, 3].add(
        -high_chord.astype(jnp.float32).reshape(rows, cols, 4, 4, NV, width)
    )
    resid = resid.at[:, :, :, :, 0].add(-wall_in.reshape(rows, cols, 4, 4, NV, width))
    return resid.reshape(rows, cols, blk, width).astype(jnp.bfloat16)


def pass_span(moving, offset):
    rim_row = moving[-1:] if offset == 1 else moving[:1]
    arrived = passed_along(rim_row, "span", offset)
    if offset == 1:
        return jnp.concatenate([arrived, moving[:-1]], 0)
    return jnp.concatenate([moving[1:], arrived], 0)


def pass_chord(moving, offset):
    rim_col = moving[:, -1:] if offset == 1 else moving[:, :1]
    arrived = passed_along(rim_col, "chord", offset)
    if offset == 1:
        return jnp.concatenate([arrived, moving[:, :-1]], 1)
    return jnp.concatenate([moving[:, 1:], arrived], 1)


def face_terms(sent):
    low_span = pass_span(sent[:, :, 0], 1)
    high_span = pass_span(sent[:, :, 1], -1)
    low_chord = pass_chord(sent[:, :, 2], 1)
    high_chord = pass_chord(sent[:, :, 3], -1)
    return (low_span, high_span, low_chord, high_chord)


def over_y(block):
    return [block] + [chord_shift(block, 0, k) for k in range(1, CY)]


def over_z(block):
    cz = lax.axis_size("chord") // CY
    return [block] + [chord_shift(block, k, 0) for k in range(1, cz)]


def per_device(adj_rhs, diag_inv, face_jac, face_mask, wall_map, couple, shell_rhs, shell_inv):
    high = lax.Precision.HIGHEST
    rows, cols, blk, width = adj_rhs.shape
    shell_count = shell_rhs.shape[0]
    size = lax.axis_size("chord")
    cz = size // CY
    chord_pos = lax.axis_index("chord")
    zpos = chord_pos // CY
    ypos = chord_pos % CY
    wall_local = wall_map.reshape(-1)
    wall_count = wall_local.shape[0]
    node = lax.iota(jnp.int32, shell_count)
    kz = lax.iota(jnp.int32, cz)[:, None]
    got_ids = ((((zpos - kz) % cz) * CY + ypos) * shell_count + node).reshape(-1)
    out_ids = ((((zpos + kz) % cz) * CY + ypos) * shell_count + node).reshape(-1)
    maps_to = [wall_local] + [chord_shift(wall_local, 0, -k) for k in range(1, CY)]
    maps_from = jnp.concatenate(over_y(wall_local))
    pick_hits = [(m[:, None] == got_ids[None, :]).astype(jnp.bfloat16) for m in maps_to]
    load_hit = (out_ids[:, None] == maps_from[None, :]).astype(jnp.bfloat16)
    fluid = jnp.einsum(
        "abmn,abnr->abmr", diag_inv, adj_rhs, preferred_element_type=jnp.float32
    ).astype(jnp.bfloat16)
    shell = jnp.einsum(
        "nst,ntr->nsr", shell_inv, shell_rhs.astype(jnp.float32), precision=high
    ).astype(jnp.bfloat16)
    weights = face_mask.astype(jnp.float32)[:, :, :, None, None]
    sdof = shell.shape[1]
    for step in range(1, ITERS):
        sent = jnp.einsum("abdmn,abnr->abdmr", face_jac, fluid, preferred_element_type=jnp.float32)
        sent = (sent * weights).astype(jnp.bfloat16)
        low_span, high_span, low_chord, high_chord = face_terms(sent)
        column = jnp.concatenate(over_z(shell.reshape(shell_count, sdof * width)))
        served = [
            jnp.dot(h, column, preferred_element_type=jnp.float32).astype(jnp.bfloat16)
            for h in pick_hits
        ]
        wall_rows = fluid.reshape(rows, cols, 4, 4, 4, NV, width)[:, :, :, :, 0].reshape(
            wall_count, NV * width
        )
        padded = jnp.pad(wall_rows, ((0, 0), (0, (sdof - NV) * width)))
        arrived = [
            chord_shift(jnp.concatenate([served[k], padded]), 0, k) for k in range(1, CY)
        ]
        picked = served[0].astype(jnp.float32)
        for a in arrived:
            picked = picked + a[:wall_count].astype(jnp.float32)
        wall_in = jnp.einsum(
            "sv,wsr->wvr", couple, picked.reshape(wall_count, sdof, width), precision=high
        )
        row_group = jnp.concatenate(
            [wall_rows] + [a[wall_count:, : NV * width] for a in arrived]
        )
        partial = jnp.dot(load_hit, row_group, preferred_element_type=jnp.float32)
        partial = partial.reshape(cz, shell_count, NV * width)
        summed = partial[0]
        for k in range(1, cz):
            summed = summed + chord_shift(partial[k], k, 0)
        shell_load = jnp.einsum(
            "sv,nvr->nsr", couple, summed.reshape(shell_count, NV, width), precision=high
        )
        resid = assemble(adj_rhs, low_span, high_span, low_chord, high_chord, wall_in)
        fluid = jnp.einsum(
            "abmn,abnr->abmr", diag_inv, resid, preferred_element_type=jnp.float32
        ).astype(jnp.bfloat16)
        shell = jnp.einsum(
            "nst,ntr->nsr", shell_inv, shell_rhs.astype(jnp.float32) - shell_load, precision=high
        ).astype(jnp.bfloat16)
    return (fluid, shell)


def solution(mesh):
    return jax.shard_map(
        per_device,
        mesh=mesh,
        in_specs=(
            P("span", "chord", None, None),
            P("span", "chord", None, None),
            P("span", "chord", None, None, None),
            P("span", "chord", None),
            P("span", "chord", None),
            P(),
            P(("span", "chord"), None, None),
            P(("span", "chord"), None, None),
        ),
        out_specs=(P("span", "chord", None, None), P(("span", "chord"), None, None)),
        check_vma=False,
    )
```

```python
import jax
import jax.numpy as jnp
from jax import lax
from jax.sharding import PartitionSpec as P

NV = 5
ITERS = 3
CY = 4


def passed_along(block, axis, distance):
    devices = range(lax.axis_size(axis))
    route = [(i - distance, i) for i in devices if i - distance in devices]
    return lax.ppermute(block, axis, route)


def chord_shift(block, dz, dy):
    size = lax.axis_size("chord")
    cz = size // CY
    route = [
        (c, ((c // CY + dz) % cz) * CY + (c % CY + dy) % CY) for c in range(size)
    ]
    return lax.ppermute(block, "chord", route)


def assemble(adj_rhs, low_span, high_span, low_chord, high_chord, wall_in):
    rows, cols, blk, width = adj_rhs.shape
    resid = adj_rhs.astype(jnp.float32).reshape(rows, cols, 4, 4, 4, NV, width)
    resid = resid.at[:, :, 0].add(
        -low_span.astype(jnp.float32).reshape(rows, cols, 4, 4, NV, width)
    )
    resid = resid.at[:, :, 3].add(
        -high_span.astype(jnp.float32).reshape(rows, cols, 4, 4, NV, width)
    )
    resid = resid.at[:, :, :, 0].add(
        -low_chord.astype(jnp.float32).reshape(rows, cols, 4, 4, NV, width)
    )
    resid = resid.at[:, :, :, 3].add(
        -high_chord.astype(jnp.float32).reshape(rows, cols, 4, 4, NV, width)
    )
    resid = resid.at[:, :, :, :, 0].add(-wall_in.reshape(rows, cols, 4, 4, NV, width))
    return resid.reshape(rows, cols, blk, width).astype(jnp.bfloat16)


def pass_span(moving, offset):
    rim_row = moving[-1:] if offset == 1 else moving[:1]
    arrived = passed_along(rim_row, "span", offset)
    if offset == 1:
        return jnp.concatenate([arrived, moving[:-1]], 0)
    return jnp.concatenate([moving[1:], arrived], 0)


def pass_chord(moving, offset):
    rim_col = moving[:, -1:] if offset == 1 else moving[:, :1]
    arrived = passed_along(rim_col, "chord", offset)
    if offset == 1:
        return jnp.concatenate([arrived, moving[:, :-1]], 1)
    return jnp.concatenate([moving[:, 1:], arrived], 1)


def face_terms(sent):
    low_span = pass_span(sent[:, :, 0], 1)
    high_span = pass_span(sent[:, :, 1], -1)
    low_chord = pass_chord(sent[:, :, 2], 1)
    high_chord = pass_chord(sent[:, :, 3], -1)
    return (low_span, high_span, low_chord, high_chord)


def over_y(block):
    return [block] + [chord_shift(block, 0, k) for k in range(1, CY)]


def over_z(block):
    cz = lax.axis_size("chord") // CY
    return [block] + [chord_shift(block, k, 0) for k in range(1, cz)]


def per_device(adj_rhs, diag_inv, face_jac, face_mask, wall_map, couple, shell_rhs, shell_inv):
    high = lax.Precision.HIGHEST
    rows, cols, blk, width = adj_rhs.shape
    shell_count = shell_rhs.shape[0]
    size = lax.axis_size("chord")
    cz = size // CY
    chord_pos = lax.axis_index("chord")
    zpos = chord_pos // CY
    ypos = chord_pos % CY
    wall_local = wall_map.reshape(-1)
    wall_count = wall_local.shape[0]
    node = lax.iota(jnp.int32, shell_count)
    kz = lax.iota(jnp.int32, cz)[:, None]
    got_ids = ((((zpos - kz) % cz) * CY + ypos) * shell_count + node).reshape(-1)
    out_ids = ((((zpos + kz) % cz) * CY + ypos) * shell_count + node).reshape(-1)
    tag = jnp.concatenate([wall_local // 32, wall_local % 32]).astype(jnp.bfloat16)
    tag = jnp.zeros((16, NV * width), jnp.bfloat16).at[0, : 2 * wall_count].set(tag)
    fluid = jnp.einsum(
        "abmn,abnr->abmr", diag_inv, adj_rhs, preferred_element_type=jnp.float32
    ).astype(jnp.bfloat16)
    shell = jnp.einsum(
        "nst,ntr->nsr", shell_inv, shell_rhs.astype(jnp.float32), precision=high
    ).astype(jnp.bfloat16)
    weights = face_mask.astype(jnp.float32)[:, :, :, None, None]
    sdof = shell.shape[1]
    for step in range(1, ITERS):
        sent = jnp.einsum("abdmn,abnr->abdmr", face_jac, fluid, preferred_element_type=jnp.float32)
        sent = (sent * weights).astype(jnp.bfloat16)
        low_span, high_span, low_chord, high_chord = face_terms(sent)
        wall_rows = fluid.reshape(rows, cols, 4, 4, 4, NV, width)[:, :, :, :, 0].reshape(
            wall_count, NV * width
        )
        if step == 1:
            arrived = over_y(jnp.concatenate([wall_rows, tag]))
            maps = [wall_local]
            for a in arrived[1:]:
                code = a[wall_count].astype(jnp.float32)
                maps.append((code[:wall_count] * 32 + code[wall_count : 2 * wall_count]).astype(jnp.int32))
            row_group = jnp.concatenate([wall_rows] + [a[:wall_count] for a in arrived[1:]])
            maps_to = [maps[0]] + [maps[CY - k] for k in range(1, CY)]
            pick_hits = [(m[:, None] == got_ids[None, :]).astype(jnp.bfloat16) for m in maps_to]
            load_hit = (out_ids[:, None] == jnp.concatenate(maps)[None, :]).astype(jnp.bfloat16)
        else:
            row_group = jnp.concatenate(over_y(wall_rows))
        column = jnp.concatenate(over_z(shell.reshape(shell_count, sdof * width)))
        served = [
            jnp.dot(h, column, preferred_element_type=jnp.float32).astype(jnp.bfloat16)
            for h in pick_hits
        ]
        picked = served[0].astype(jnp.float32)
        for k in range(1, CY):
            picked = picked + chord_shift(served[k], 0, k).astype(jnp.float32)
        wall_in = jnp.einsum(
            "sv,wsr->wvr", couple, picked.reshape(wall_count, sdof, width), precision=high
        )
        partial = jnp.dot(load_hit, row_group, preferred_element_type=jnp.float32)
        partial = partial.reshape(cz, shell_count, NV * width)
        summed = partial[0]
        for k in range(1, cz):
            summed = summed + chord_shift(partial[k], k, 0)
        shell_load = jnp.einsum(
            "sv,nvr->nsr", couple, summed.reshape(shell_count, NV, width), precision=high
        )
        resid = assemble(adj_rhs, low_span, high_span, low_chord, high_chord, wall_in)
        fluid = jnp.einsum(
            "abmn,abnr->abmr", diag_inv, resid, preferred_element_type=jnp.float32
        ).astype(jnp.bfloat16)
        shell = jnp.einsum(
            "nst,ntr->nsr", shell_inv, shell_rhs.astype(jnp.float32) - shell_load, precision=high
        ).astype(jnp.bfloat16)
    return (fluid, shell)


def solution(mesh):
    return jax.shard_map(
        per_device,
        mesh=mesh,
        in_specs=(
            P("span", "chord", None, None),
            P("span", "chord", None, None),
            P("span", "chord", None, None, None),
            P("span", "chord", None),
            P("span", "chord", None),
            P(),
            P(("span", "chord"), None, None),
            P(("span", "chord"), None, None),
        ),
        out_specs=(P("span", "chord", None, None), P(("span", "chord"), None, None)),
        check_vma=False,
    )
```
